256 devices in a mesh: lag: 4 (over y_lo, core), recv: 8 (over z), src: 8 (over y_hi, x).
Axes of the slice: x: 4, y: 4 (y_hi: 2, y_lo: 2; y = y_hi * 2 + y_lo), z: 8, core: 2. Of those that a mesh axis runs over, the one named last changes fastest.
Arguments:
- kernel: bfloat16 [4096, 32, 4096], P('recv', 'lag', 'src'), may hold values from -0.0234375 to 0.0234375
- causal_mask: int32 [32, 32, 32], P('recv', 'lag', 'src'), may hold values from 0 to 1, as said below
- history: bfloat16 [32, 4096, 256], P('lag', 'src'), may hold values from -4 to 4
- background: float32 [4096, 256], P('recv'), may hold values from -6 to 6
- classes: int32 [4096], P('recv'), may hold values from 0 to 7
- rate_scale: float32 [8], replicated, may hold values from 0.5 to 2
- stress_scale: float32 [8], replicated, may hold values from 0.5 to 2
Outputs:
- rates: bfloat16 [3, 4096, 256], P(None, 'recv')
The draws below stay inside these ranges and needn't reach their ends.
Inputs may be any that keep to these rules, and one draw needn't show every extreme that they name: causal_mask[p, l, q] is 1 exactly when |p - q| <= r_l for a whole number r_l that never falls as l grows.
All inputs are finite; a program needn't handle non-finite values.
Results may differ from the reference program's by a relative error of at most 0.0019.
Values may be sent and summed in bfloat16 or wider, within the bound.
No kernel may reach another device: no remote copies, remote signals or barrier semaphores. Data moves between devices by JAX's collectives and lax.ppermute only.
A program may use at most 64 MiB of HBM per device.

```python
import math
import jax
import jax.numpy as jnp
from jax import lax

E = 4096
BLK = 128
S = 256
STEPS = 3
NCLASS = 8
LAGS = 32
NB = 32


def draw_causal_mask(key, part):
    reach = NB // 2 + jnp.cumsum(jax.random.randint(key, (LAGS,), 0, 3))
    blocks = jnp.arange(NB, dtype=jnp.int32)
    apart = jnp.abs(blocks[:, None, None] - blocks[None, None, :])
    return (apart <= reach[None, :, None]).astype(jnp.int32)


def touch_ends(array, key, smallest, top_value):
    place = [jax.random.randint(jax.random.fold_in(key, axis), (), 0, length) for axis, length in enumerate(array.shape)]
    widest = array.shape.index(max(array.shape))
    beside = place[:widest] + [(place[widest] + 1) % array.shape[widest]] + place[widest + 1:]
    return array.at[tuple(place)].set(smallest).at[tuple(beside)].set(top_value)


def block_scale(own_key, shape, cuts, smallest, largest):
    factor_of, own = 1.0, jax.random.fold_in(own_key, 6)
    for axis_at, parts in cuts:
        steps = jnp.exp(jax.random.uniform(jax.random.fold_in(own, axis_at), (parts,), jnp.float32, smallest / len(cuts), largest / len(cuts)))
        factor_of = factor_of * jnp.repeat(steps, shape[axis_at] // parts).reshape([-1 if axis == axis_at else 1 for axis in range(len(shape))])
    return factor_of


def gaussian(rng, extent, scale, bound, split=(), kind=jnp.bfloat16):
    drawn = jax.random.normal(rng, extent, jnp.float32) * scale
    if len(split) > 0:
        drawn = block_scale(rng, extent, split, -0.22, 0.18) * drawn
    return jnp.clip(drawn, min=-bound, max=bound).astype(kind)


def setup_inputs(seed: int = 0) -> dict:
    splits = jax.random.split(jax.random.key(seed), 8)
    return {
        "kernel": gaussian(splits[0], (E, LAGS, E), (E * LAGS // 2) ** -0.5, 0.0234375, ((0, 8), (1, 4), (2, 8))),
        "causal_mask": draw_causal_mask(jax.random.fold_in(splits[7], 71), 0),
        "history": gaussian(splits[2], (LAGS, E, S), 0.7, 4.0, ((0, 4), (1, 8))),
        "background": gaussian(splits[3], (E, S), 1.0, 6.0, ((0, 8),), jnp.float32),
        "classes": touch_ends(jax.random.randint(splits[4], (E,), 0, NCLASS), jax.random.fold_in(splits[4], 1), 0, NCLASS - 1).astype(jnp.int32),
        "rate_scale": jnp.clip(jnp.exp(jax.random.uniform(splits[5], (NCLASS,), jnp.float32, math.log(0.5), math.log(2.0))), 0.5, 2.0),
        "stress_scale": jnp.clip(jnp.exp(jax.random.uniform(splits[6], (NCLASS,), jnp.float32, math.log(0.5), math.log(2.0))), 0.5, 2.0),
    }


def stress_field(kernel, causal_mask, history):
    def add_lag(summed, lag_pos):
        block = lax.dynamic_index_in_dim(kernel, lag_pos, 1, keepdims=False)
        allowed = lax.dynamic_index_in_dim(causal_mask, lag_pos, 1, keepdims=False)
        allowed = jnp.repeat(jnp.repeat(allowed, BLK, 0), BLK, 1) > 0
        block = jnp.where(allowed, block, jnp.zeros_like(block)).astype(jnp.float32)
        past = lax.dynamic_index_in_dim(history, lag_pos, 0, keepdims=False).astype(jnp.float32)
        product = jnp.dot(block, past, precision=lax.Precision.HIGHEST, preferred_element_type=jnp.float32)
        return summed + product, None

    summed, unused = lax.scan(add_lag, jnp.zeros((E, S), jnp.float32), jnp.arange(LAGS, dtype=jnp.int32))
    return summed


def reference(kernel, causal_mask, history, background, classes, rate_scale, stress_scale):
    limit = rate_scale[classes][:, None]
    width_scale = stress_scale[classes][:, None]
    produced = []
    for step_index in range(STEPS):
        stress = stress_field(kernel, causal_mask, history)
        new_rates = (limit * jnp.tanh((background + stress) / width_scale)).astype(jnp.bfloat16)
        produced.append(new_rates)
        history = jnp.concatenate([new_rates[None], history[:-1]], axis=0)
    return jnp.stack(produced)
```

```python
import jax
import jax.numpy as jnp
from jax import lax
from jax.sharding import PartitionSpec as P

STEPS = 3


def swap(block, axis, mask):
    size = lax.axis_size(axis)
    return lax.ppermute(block, axis, [(i, i ^ mask) for i in range(size)])


def tree_stages():
    stages = []
    for axis in ("lag", "src"):
        mask = 1
        while mask < lax.axis_size(axis):
            stages.append((axis, mask))
            mask *= 2
    return stages


def reduce_scatter(x, stages):
    offset = 0
    for axis, mask in stages:
        half = x.shape[0] // 2
        bit = (lax.axis_index(axis) // mask) % 2
        keep = lax.dynamic_slice_in_dim(x, bit * half, half, 0)
        send = lax.dynamic_slice_in_dim(x, (1 - bit) * half, half, 0)
        x = keep + swap(send, axis, mask)
        offset = offset + bit * half
    return x, offset


def all_gather(y, stages):
    for axis, mask in reversed(stages):
        bit = (lax.axis_index(axis) // mask) % 2
        other = swap(y, axis, mask)
        first = jnp.where(bit == 0, y, other)
        second = jnp.where(bit == 0, other, y)
        y = jnp.concatenate([first, second], axis=0)
    return y


def friction(stress, offset, background, classes, rate_scale, stress_scale):
    row_total = stress.shape[0]
    element_class = lax.dynamic_slice_in_dim(classes, offset, row_total, 0)
    loaded = lax.dynamic_slice_in_dim(background, offset, row_total, 0)
    selector = (
        element_class[:, None] == jnp.arange(rate_scale.shape[0], dtype=jnp.int32)[None, :]
    ).astype(jnp.float32)
    limit = jnp.sum(selector * rate_scale[None, :], axis=1)[:, None]
    width_scale = jnp.sum(selector * stress_scale[None, :], axis=1)[:, None]
    return (limit * jnp.tanh((loaded + stress) / width_scale)).astype(jnp.bfloat16)


def newest_to_sources(new_rates):
    recv_n = lax.axis_size("recv")
    src_n = lax.axis_size("src")
    route = [(s * src_n + r, r * src_n + s) for r in range(recv_n) for s in range(src_n)]
    return lax.ppermute(new_rates, ("lag", "recv", "src"), route)


def aged_from_previous(oldest):
    n = lax.axis_size("lag")
    return lax.ppermute(oldest, "lag", [(i, i + 1) for i in range(n - 1)])


def local(kernel, causal_mask, history, background, classes, rate_scale, stress_scale):
    rows_here, lag_here, cols_here = kernel.shape
    block_size = rows_here // causal_mask.shape[0]
    allowed = jnp.repeat(jnp.repeat(causal_mask, block_size, 0), block_size, 2) > 0
    masked_rows = jnp.where(allowed, kernel, jnp.zeros_like(kernel)).reshape(
        rows_here, lag_here * cols_here
    )
    lag_pos = lax.axis_index("lag")
    scenarios = history.shape[2]
    stages = tree_stages()
    produced = []
    for step_index in range(STEPS):
        stacked = history.reshape(lag_here * cols_here, scenarios)
        partial = jnp.dot(masked_rows, stacked, preferred_element_type=jnp.float32)
        share_rows, offset = reduce_scatter(partial, stages)
        local_rates = friction(share_rows, offset, background, classes, rate_scale, stress_scale)
        new_rates = all_gather(local_rates, stages)
        produced.append(new_rates)
        if step_index + 1 < STEPS:
            newest = newest_to_sources(new_rates)
            aged_block = aged_from_previous(history[-1])
            incoming = jnp.where(lag_pos == 0, newest, aged_block)
            history = jnp.concatenate([incoming[None], history[:-1]], axis=0)
    return jnp.stack(produced)


def solution(mesh):
    in_specs = (
        P("recv", "lag", "src"),
        P("recv", "lag", "src"),
        P("lag", "src", None),
        P("recv", None),
        P("recv"),
        P(),
        P(),
    )
    out_specs = P(None, "recv", None)
    return jax.shard_map(local, mesh=mesh, in_specs=in_specs, out_specs=out_specs, check_vma=False)
```

```python
import jax
import jax.numpy as jnp
from jax import lax
from jax.sharding import PartitionSpec as P

STEPS = 3


def shifted(block, axis, shift):
    size = lax.axis_size(axis)
    return lax.ppermute(block, axis, [(i, (i + shift) % size) for i in range(size)])


def reduce_scatter(x, axes):
    offset = 0
    for axis in axes:
        n = lax.axis_size(axis)
        part = x.shape[0] // n
        me = lax.axis_index(axis)
        total = lax.dynamic_slice_in_dim(x, me * part, part, 0)
        for shift in range(1, n):
            send = lax.dynamic_slice_in_dim(x, ((me + shift) % n) * part, part, 0)
            total = total + shifted(send, axis, shift)
        x = total
        offset = offset + me * part
    return x, offset


def all_gather(y, axes):
    for axis in reversed(axes):
        n = lax.axis_size(axis)
        me = lax.axis_index(axis)
        pieces = [y] + [shifted(y, axis, -shift) for shift in range(1, n)]
        ring = jnp.concatenate(pieces + pieces, axis=0)
        y = lax.dynamic_slice_in_dim(ring, ((n - me) % n) * y.shape[0], n * y.shape[0], 0)
    return y


def friction(stress, offset, background, classes, rate_scale, stress_scale):
    row_total = stress.shape[0]
    element_class = lax.dynamic_slice_in_dim(classes, offset, row_total, 0)
    loaded = lax.dynamic_slice_in_dim(background, offset, row_total, 0)
    selector = (
        element_class[:, None] == jnp.arange(rate_scale.shape[0], dtype=jnp.int32)[None, :]
    ).astype(jnp.float32)
    limit = jnp.sum(selector * rate_scale[None, :], axis=1)[:, None]
    width_scale = jnp.sum(selector * stress_scale[None, :], axis=1)[:, None]
    return (limit * jnp.tanh((loaded + stress) / width_scale)).astype(jnp.bfloat16)


def newest_to_sources(new_rates):
    recv_n = lax.axis_size("recv")
    src_n = lax.axis_size("src")
    route = [(s * src_n + r, r * src_n + s) for r in range(recv_n) for s in range(src_n)]
    return lax.ppermute(new_rates, ("lag", "recv", "src"), route)


def aged_from_previous(oldest):
    n = lax.axis_size("lag")
    return lax.ppermute(oldest, "lag", [(i, i + 1) for i in range(n - 1)])


def local(kernel, causal_mask, history, background, classes, rate_scale, stress_scale):
    rows_here, lag_here, cols_here = kernel.shape
    block_size = rows_here // causal_mask.shape[0]
    allowed = jnp.repeat(jnp.repeat(causal_mask, block_size, 0), block_size, 2) > 0
    masked_rows = jnp.where(allowed, kernel, jnp.zeros_like(kernel)).reshape(
        rows_here, lag_here * cols_here
    )
    lag_pos = lax.axis_index("lag")
    scenarios = history.shape[2]
    stages = ("lag", "src")
    produced = []
    for step_index in range(STEPS):
        stacked = history.reshape(lag_here * cols_here, scenarios)
        partial = jnp.dot(masked_rows, stacked, preferred_element_type=jnp.float32)
        share_rows, offset = reduce_scatter(partial, stages)
        local_rates = friction(share_rows, offset, background, classes, rate_scale, stress_scale)
        new_rates = all_gather(local_rates, stages)
        produced.append(new_rates)
        if step_index + 1 < STEPS:
            newest = newest_to_sources(new_rates)
            aged_block = aged_from_previous(history[-1])
            incoming = jnp.where(lag_pos == 0, newest, aged_block)
            history = jnp.concatenate([incoming[None], history[:-1]], axis=0)
    return jnp.stack(produced)


def solution(mesh):
    in_specs = (
        P("recv", "lag", "src"),
        P("recv", "lag", "src"),
        P("lag", "src", None),
        P("recv", None),
        P("recv"),
        P(),
        P(),
    )
    out_specs = P(None, "recv", None)
    return jax.shard_map(local, mesh=mesh, in_specs=in_specs, out_specs=out_specs, check_vma=False)
```

```python
import jax
import jax.numpy as jnp
from jax import lax
from jax.sharding import PartitionSpec as P

STEPS = 3


def swap_src(block, mask):
    size = lax.axis_size("src")
    route = [(i, i ^ mask) for i in range(size)]
    return lax.ppermute(block, ("lag", "src"), route)


def bit_masks(axis):
    masks = []
    mask = 1
    while mask < lax.axis_size(axis):
        masks.append(mask)
        mask *= 2
    return masks


def reduce_scatter_src(x):
    offset = 0
    for mask in bit_masks("src"):
        half = x.shape[0] // 2
        bit = (lax.axis_index("src") // mask) % 2
        keep = lax.dynamic_slice_in_dim(x, bit * half, half, 0)
        send = lax.dynamic_slice_in_dim(x, (1 - bit) * half, half, 0)
        x = keep + swap_src(send, mask)
        offset = offset + bit * half
    return x, offset


def all_gather_src(y):
    for mask in reversed(bit_masks("src")):
        bit = (lax.axis_index("src") // mask) % 2
        other = swap_src(y, mask)
        first = jnp.where(bit == 0, y, other)
        second = jnp.where(bit == 0, other, y)
        y = jnp.concatenate([first, second], axis=0)
    return y


def reduce_to_lag0(x):
    n = lax.axis_size("lag")
    for mask in bit_masks("lag"):
        route = [(i, i - mask) for i in range(n) if i % (2 * mask) == mask]
        x = x + lax.ppermute(x, "lag", route)
    return x


def broadcast_from_lag0(x):
    n = lax.axis_size("lag")
    pos = lax.axis_index("lag")
    for mask in reversed(bit_masks("lag")):
        route = [(i, i + mask) for i in range(n) if i % (2 * mask) == 0]
        arrived = lax.ppermute(x, "lag", route)
        x = jnp.where(pos % (2 * mask) == mask, arrived, x)
    return x


def to_sources(rates_block):
    recv_n = lax.axis_size("recv")
    src_n = lax.axis_size("src")
    route = [(s * src_n + r, r * src_n + s) for r in range(recv_n) for s in range(src_n)]
    return lax.ppermute(rates_block, ("lag", "recv", "src"), route)


def friction(stress, offset, background, classes, rate_scale, stress_scale):
    row_total = stress.shape[0]
    element_class = lax.dynamic_slice_in_dim(classes, offset, row_total, 0)
    loaded = lax.dynamic_slice_in_dim(background, offset, row_total, 0)
    selector = (
        element_class[:, None] == jnp.arange(rate_scale.shape[0], dtype=jnp.int32)[None, :]
    ).astype(jnp.float32)
    limit = jnp.sum(selector * rate_scale[None, :], axis=1)[:, None]
    width_scale = jnp.sum(selector * stress_scale[None, :], axis=1)[:, None]
    return (limit * jnp.tanh((loaded + stress) / width_scale)).astype(jnp.bfloat16)


def local(kernel, causal_mask, history, background, classes, rate_scale, stress_scale):
    rows_here, lag_here, cols_here = kernel.shape
    block_size = rows_here // causal_mask.shape[0]
    allowed = jnp.repeat(jnp.repeat(causal_mask, block_size, 0), block_size, 2) > 0
    masked = jnp.where(allowed, kernel, jnp.zeros_like(kernel))
    masked_rows = masked.reshape(rows_here, lag_here * cols_here)
    scenarios = history.shape[2]
    lag_n = lax.axis_size("lag")

    def rates_of(partial):
        share, offset = reduce_scatter_src(partial)
        return all_gather_src(friction(share, offset, background, classes, rate_scale, stress_scale))

    ahead = STEPS - 1
    earlier = lax.ppermute(history[lag_here - ahead:], "lag", [(i, i + 1) for i in range(lag_n - 1)])
    extended = jnp.concatenate([earlier, history], axis=0)
    first = jnp.dot(masked_rows, history.reshape(lag_here * cols_here, scenarios),
                    preferred_element_type=jnp.float32)
    later = []
    for step_index in range(1, STEPS):
        shifted = extended[ahead - step_index: ahead - step_index + lag_here]
        later.append(jnp.dot(masked_rows, shifted.reshape(lag_here * cols_here, scenarios),
                             preferred_element_type=jnp.float32))
    later = reduce_to_lag0(jnp.concatenate(later, axis=1))

    produced = [rates_of(reduce_to_lag0(first))]
    sources = []
    for step_index in range(1, STEPS):
        sources.append(to_sources(produced[-1]))
        partial = later[:, (step_index - 1) * scenarios: step_index * scenarios]
        for lag_pos in range(step_index):
            partial = partial + jnp.dot(masked[:, lag_pos, :], sources[step_index - 1 - lag_pos],
                                        preferred_element_type=jnp.float32)
        produced.append(rates_of(partial))
    return jnp.stack([broadcast_from_lag0(r) for r in produced])


def solution(mesh):
    in_specs = (
        P("recv", "lag", "src"),
        P("recv", "lag", "src"),
        P("lag", "src", None),
        P("recv", None),
        P("recv"),
        P(),
        P(),
    )
    out_specs = P(None, "recv", None)
    return jax.shard_map(local, mesh=mesh, in_specs=in_specs, out_specs=out_specs, check_vma=False)
```

```python
import jax
import jax.numpy as jnp
from jax import lax
from jax.sharding import PartitionSpec as P

STEPS = 3


def bit_masks(axis):
    masks = []
    mask = 1
    while mask < lax.axis_size(axis):
        masks.append(mask)
        mask *= 2
    return masks


def swap(block, axis, mask):
    size = lax.axis_size(axis)
    return lax.ppermute(block, axis, [(i, i ^ mask) for i in range(size)])


def reduce_scatter_lag(x):
    offset = 0
    for mask in bit_masks("lag"):
        half = x.shape[0] // 2
        bit = (lax.axis_index("lag") // mask) % 2
        keep = lax.dynamic_slice_in_dim(x, bit * half, half, 0)
        send = lax.dynamic_slice_in_dim(x, (1 - bit) * half, half, 0)
        x = keep + swap(send, "lag", mask)
        offset = offset + bit * half
    return x, offset


def all_reduce_src(x):
    for mask in bit_masks("src"):
        x = x + swap(x, "src", mask)
    return x


def all_gather_lag(y):
    for mask in reversed(bit_masks("lag")):
        bit = (lax.axis_index("lag") // mask) % 2
        other = swap(y, "lag", mask)
        first = jnp.where(bit == 0, y, other)
        second = jnp.where(bit == 0, other, y)
        y = jnp.concatenate([first, second], axis=0)
    return y


def to_sources(rates_block):
    recv_n = lax.axis_size("recv")
    src_n = lax.axis_size("src")
    route = [(s * src_n + r, r * src_n + s) for r in range(recv_n) for s in range(src_n)]
    return lax.ppermute(rates_block, ("lag", "recv", "src"), route)


def friction(stress, offset, background, classes, rate_scale, stress_scale):
    row_total = stress.shape[0]
    element_class = lax.dynamic_slice_in_dim(classes, offset, row_total, 0)
    loaded = lax.dynamic_slice_in_dim(background, offset, row_total, 0)
    selector = (
        element_class[:, None] == jnp.arange(rate_scale.shape[0], dtype=jnp.int32)[None, :]
    ).astype(jnp.float32)
    limit = jnp.sum(selector * rate_scale[None, :], axis=1)[:, None]
    width_scale = jnp.sum(selector * stress_scale[None, :], axis=1)[:, None]
    return (limit * jnp.tanh((loaded + stress) / width_scale)).astype(jnp.bfloat16)


def local(kernel, causal_mask, history, background, classes, rate_scale, stress_scale):
    rows_here, lag_here, cols_here = kernel.shape
    block_size = rows_here // causal_mask.shape[0]
    allowed = jnp.repeat(jnp.repeat(causal_mask, block_size, 0), block_size, 2) > 0
    masked_rows = jnp.where(allowed, kernel, jnp.zeros_like(kernel)).reshape(
        rows_here, lag_here * cols_here
    )
    scenarios = history.shape[2]
    lag_n = lax.axis_size("lag")

    def rates_of(partial):
        share, offset = reduce_scatter_lag(partial)
        total = all_reduce_src(share)
        return all_gather_lag(friction(total, offset, background, classes, rate_scale, stress_scale))

    ahead = STEPS - 1
    earlier = lax.ppermute(history[lag_here - ahead:], "lag", [(i, i + 1) for i in range(lag_n - 1)])
    extended = jnp.concatenate([earlier, history], axis=0)
    known = [jnp.dot(masked_rows, history.reshape(lag_here * cols_here, scenarios),
                     preferred_element_type=jnp.float32)]
    for step_index in range(1, STEPS):
        shifted = extended[ahead - step_index: ahead - step_index + lag_here]
        known.append(jnp.dot(masked_rows, shifted.reshape(lag_here * cols_here, scenarios),
                             preferred_element_type=jnp.float32))

    produced = [rates_of(known[0])]
    sources = []
    for step_index in range(1, STEPS):
        sources.append(to_sources(produced[-1]))
        partial = known[step_index]
        for lag_pos in range(step_index):
            partial = partial + jnp.dot(
                masked_rows[:, lag_pos * cols_here: (lag_pos + 1) * cols_here],
                sources[step_index - 1 - lag_pos],
                preferred_element_type=jnp.float32,
            )
        produced.append(rates_of(partial))
    return jnp.stack(produced)


def solution(mesh):
    in_specs = (
        P("recv", "lag", "src"),
        P("recv", "lag", "src"),
        P("lag", "src", None),
        P("recv", None),
        P("recv"),
        P(),
        P(),
    )
    out_specs = P(None, "recv", None)
    return jax.shard_map(local, mesh=mesh, in_specs=in_specs, out_specs=out_specs, check_vma=False)
```

```python
import jax
import jax.numpy as jnp
from jax import lax
from jax.sharding import PartitionSpec as P

STEPS = 3
SERIAL = 2


def bit_masks(axis):
    masks = []
    mask = 1
    while mask < lax.axis_size(axis):
        masks.append(mask)
        mask *= 2
    return masks


def swap(block, axis, mask):
    size = lax.axis_size(axis)
    return lax.ppermute(block, axis, [(i, i ^ mask) for i in range(size)])


def chunk_offset(lag_pos, rows):
    offset = 0
    for mask in bit_masks("lag"):
        rows = rows // 2
        offset = offset + ((lag_pos // mask) % 2) * rows
    return offset


def reduce_scatter_lag(x):
    for mask in bit_masks("lag"):
        half = x.shape[0] // 2
        bit = (lax.axis_index("lag") // mask) % 2
        keep = lax.dynamic_slice_in_dim(x, bit * half, half, 0)
        send = lax.dynamic_slice_in_dim(x, (1 - bit) * half, half, 0)
        x = keep + swap(send, "lag", mask)
    return x


def all_reduce_src(x):
    for mask in bit_masks("src"):
        x = x + swap(x, "src", mask)
    return x


def all_gather_lag(y):
    for mask in reversed(bit_masks("lag")):
        bit = (lax.axis_index("lag") // mask) % 2
        other = swap(y, "lag", mask)
        first = jnp.where(bit == 0, y, other)
        second = jnp.where(bit == 0, other, y)
        y = jnp.concatenate([first, second], axis=0)
    return y


def transposed(chunk):
    recv_n = lax.axis_size("recv")
    src_n = lax.axis_size("src")
    route = [(s * src_n + r, r * src_n + s) for r in range(recv_n) for s in range(src_n)]
    return lax.ppermute(chunk, ("recv", "src"), route)


def friction(stress, offset, background, classes, rate_scale, stress_scale):
    row_total = stress.shape[0]
    element_class = lax.dynamic_slice_in_dim(classes, offset, row_total, 0)
    loaded = lax.dynamic_slice_in_dim(background, offset, row_total, 0)
    selector = (
        element_class[:, None] == jnp.arange(rate_scale.shape[0], dtype=jnp.int32)[None, :]
    ).astype(jnp.float32)
    limit = jnp.sum(selector * rate_scale[None, :], axis=1)[:, None]
    width_scale = jnp.sum(selector * stress_scale[None, :], axis=1)[:, None]
    return (limit * jnp.tanh((loaded + stress) / width_scale)).astype(jnp.bfloat16)


def local(kernel, causal_mask, history, background, classes, rate_scale, stress_scale):
    rows_here, lag_here, cols_here = kernel.shape
    block_size = rows_here // causal_mask.shape[0]
    allowed = jnp.repeat(jnp.repeat(causal_mask, block_size, 0), block_size, 2) > 0
    masked_rows = jnp.where(allowed, kernel, jnp.zeros_like(kernel)).reshape(
        rows_here, lag_here * cols_here
    )
    scenarios = history.shape[2]
    lag_n = lax.axis_size("lag")
    lag_pos = lax.axis_index("lag")
    chunk_rows = rows_here // lag_n
    offset = chunk_offset(lag_pos, rows_here)

    serial = []
    for lag_index in range(SERIAL):
        allowed_here = jnp.repeat(jnp.repeat(causal_mask[:, lag_index, :], block_size, 0), block_size, 1) > 0
        serial.append(jnp.where(allowed_here, kernel[:, lag_index, :], jnp.zeros_like(kernel[:, lag_index, :])))
    serial = jnp.stack(serial)
    own = lax.dynamic_slice_in_dim(serial, offset, chunk_rows, 1)
    for target in range(1, lag_n):
        start = chunk_offset(target, rows_here)
        arrived = lax.ppermute(serial[:, start:start + chunk_rows], "lag", [(0, target)])
        own = jnp.where(lag_pos == target, arrived, own)

    ahead = STEPS - 1
    earlier = lax.ppermute(history[lag_here - ahead:], "lag", [(i, i + 1) for i in range(lag_n - 1)])
    extended = jnp.concatenate([earlier, history], axis=0)
    first = jnp.dot(masked_rows, history.reshape(lag_here * cols_here, scenarios),
                    preferred_element_type=jnp.float32)
    later = []
    for step_index in range(1, STEPS):
        shifted = extended[ahead - step_index: ahead - step_index + lag_here]
        later.append(jnp.dot(masked_rows, shifted.reshape(lag_here * cols_here, scenarios),
                             preferred_element_type=jnp.float32))
    later = reduce_scatter_lag(jnp.concatenate(later, axis=1))
    known = [reduce_scatter_lag(first)] + [
        later[:, (t - 1) * scenarios: t * scenarios] for t in range(1, STEPS)
    ]

    outputs = []
    sources = []
    for step_index in range(STEPS):
        partial = known[step_index]
        for lag_index in range(min(step_index, SERIAL)):
            partial = partial + jnp.dot(own[lag_index], sources[step_index - 1 - lag_index],
                                        preferred_element_type=jnp.float32)
        total = all_reduce_src(partial)
        rates_chunk = friction(total, offset, background, classes, rate_scale, stress_scale)
        if step_index + 1 < STEPS:
            block = all_gather_lag(transposed(rates_chunk))
            sources.append(block)
        outputs.append(all_gather_lag(rates_chunk))
    return jnp.stack(outputs)


def solution(mesh):
    in_specs = (
        P("recv", "lag", "src"),
        P("recv", "lag", "src"),
        P("lag", "src", None),
        P("recv", None),
        P("recv"),
        P(),
        P(),
    )
    out_specs = P(None, "recv", None)
    return jax.shard_map(local, mesh=mesh, in_specs=in_specs, out_specs=out_specs, check_vma=False)
```

```python
import jax
import jax.numpy as jnp
from jax import lax
from jax.sharding import PartitionSpec as P

STEPS = 3
SERIAL = 2


def bit_masks(axis):
    masks = []
    mask = 1
    while mask < lax.axis_size(axis):
        masks.append(mask)
        mask *= 2
    return masks


def swap(block, axis, mask):
    size = lax.axis_size(axis)
    return lax.ppermute(block, axis, [(i, i ^ mask) for i in range(size)])


def chunk_offset(lag_pos, rows):
    offset = 0
    for mask in bit_masks("lag"):
        rows = rows // 2
        offset = offset + ((lag_pos // mask) % 2) * rows
    return offset


def reduce_scatter_lag(x):
    for mask in bit_masks("lag"):
        half = x.shape[0] // 2
        bit = (lax.axis_index("lag") // mask) % 2
        keep = lax.dynamic_slice_in_dim(x, bit * half, half, 0)
        send = lax.dynamic_slice_in_dim(x, (1 - bit) * half, half, 0)
        x = keep + swap(send, "lag", mask)
    return x


def all_reduce_src(x):
    for mask in bit_masks("src"):
        x = x + swap(x, "src", mask)
    return x


def all_gather_lag(y):
    for mask in reversed(bit_masks("lag")):
        bit = (lax.axis_index("lag") // mask) % 2
        other = swap(y, "lag", mask)
        first = jnp.where(bit == 0, y, other)
        second = jnp.where(bit == 0, other, y)
        y = jnp.concatenate([first, second], axis=0)
    return y


def ring_distance(a, b, size):
    d = abs(a - b) % size
    return min(d, size - d)


def src_distance(a, b):
    x_size = 4
    hops_x = ring_distance(a % x_size, b % x_size, x_size)
    hops_y = 2 * ring_distance(a // x_size, b // x_size, 2)
    return hops_x + hops_y


def transposed(chunk):
    recv_n = lax.axis_size("recv")
    src_n = lax.axis_size("src")
    route = []
    for s in range(src_n):
        far_first = sorted(range(recv_n), key=lambda r: (-ring_distance(r, s, recv_n), r))
        near_first = sorted(range(src_n), key=lambda q: (src_distance(q, s), q))
        for r, sender in zip(far_first, near_first):
            route.append((s * src_n + sender, r * src_n + s))
    return lax.ppermute(chunk, ("recv", "src"), route)


def friction(stress, offset, background, classes, rate_scale, stress_scale):
    row_total = stress.shape[0]
    element_class = lax.dynamic_slice_in_dim(classes, offset, row_total, 0)
    loaded = lax.dynamic_slice_in_dim(background, offset, row_total, 0)
    selector = (
        element_class[:, None] == jnp.arange(rate_scale.shape[0], dtype=jnp.int32)[None, :]
    ).astype(jnp.float32)
    limit = jnp.sum(selector * rate_scale[None, :], axis=1)[:, None]
    width_scale = jnp.sum(selector * stress_scale[None, :], axis=1)[:, None]
    return (limit * jnp.tanh((loaded + stress) / width_scale)).astype(jnp.bfloat16)


def local(kernel, causal_mask, history, background, classes, rate_scale, stress_scale):
    rows_here, lag_here, cols_here = kernel.shape
    block_size = rows_here // causal_mask.shape[0]
    allowed = jnp.repeat(jnp.repeat(causal_mask, block_size, 0), block_size, 2) > 0
    masked_rows = jnp.where(allowed, kernel, jnp.zeros_like(kernel)).reshape(
        rows_here, lag_here * cols_here
    )
    scenarios = history.shape[2]
    lag_n = lax.axis_size("lag")
    lag_pos = lax.axis_index("lag")
    chunk_rows = rows_here // lag_n
    offset = chunk_offset(lag_pos, rows_here)

    serial = []
    for lag_index in range(SERIAL):
        allowed_here = jnp.repeat(jnp.repeat(causal_mask[:, lag_index, :], block_size, 0), block_size, 1) > 0
        serial.append(jnp.where(allowed_here, kernel[:, lag_index, :], jnp.zeros_like(kernel[:, lag_index, :])))
    serial = jnp.stack(serial)
    own = lax.dynamic_slice_in_dim(serial, offset, chunk_rows, 1)
    for target in range(1, lag_n):
        start = chunk_offset(target, rows_here)
        arrived = lax.ppermute(serial[:, start:start + chunk_rows], "lag", [(0, target)])
        own = jnp.where(lag_pos == target, arrived, own)

    ahead = STEPS - 1
    earlier = lax.ppermute(history[lag_here - ahead:], "lag", [(i, i + 1) for i in range(lag_n - 1)])
    extended = jnp.concatenate([earlier, history], axis=0)
    first = jnp.dot(masked_rows, history.reshape(lag_here * cols_here, scenarios),
                    preferred_element_type=jnp.float32)
    later = []
    for step_index in range(1, STEPS):
        shifted = extended[ahead - step_index: ahead - step_index + lag_here]
        later.append(jnp.dot(masked_rows, shifted.reshape(lag_here * cols_here, scenarios),
                             preferred_element_type=jnp.float32))
    later = reduce_scatter_lag(jnp.concatenate(later, axis=1))
    known = [reduce_scatter_lag(first)] + [
        later[:, (t - 1) * scenarios: t * scenarios] for t in range(1, STEPS)
    ]

    outputs = []
    sources = []
    for step_index in range(STEPS):
        partial = known[step_index]
        for lag_index in range(min(step_index, SERIAL)):
            partial = partial + jnp.dot(own[lag_index], sources[step_index - 1 - lag_index],
                                        preferred_element_type=jnp.float32)
        total = all_reduce_src(partial)
        rates_chunk = friction(total, offset, background, classes, rate_scale, stress_scale)
        if step_index + 1 < STEPS:
            block = all_gather_lag(transposed(rates_chunk))
            sources.append(block)
        outputs.append(all_gather_lag(rates_chunk))
    return jnp.stack(outputs)


def solution(mesh):
    in_specs = (
        P("recv", "lag", "src"),
        P("recv", "lag", "src"),
        P("lag", "src", None),
        P("recv", None),
        P("recv"),
        P(),
        P(),
    )
    out_specs = P(None, "recv", None)
    return jax.shard_map(local, mesh=mesh, in_specs=in_specs, out_specs=out_specs, check_vma=False)
```

```python
import jax
import jax.numpy as jnp
from jax import lax
from jax.sharding import PartitionSpec as P

STEPS = 3
SERIAL = 2


def bit_masks(axis):
    masks = []
    mask = 1
    while mask < lax.axis_size(axis):
        masks.append(mask)
        mask *= 2
    return masks


def swap(block, axis, mask):
    size = lax.axis_size(axis)
    return lax.ppermute(block, axis, [(i, i ^ mask) for i in range(size)])


def chunk_offset(lag_pos, rows):
    offset = 0
    for mask in bit_masks("lag"):
        rows = rows // 2
        offset = offset + ((lag_pos // mask) % 2) * rows
    return offset


def reduce_scatter_lag(x):
    for mask in bit_masks("lag"):
        half = x.shape[0] // 2
        bit = (lax.axis_index("lag") // mask) % 2
        keep = lax.dynamic_slice_in_dim(x, bit * half, half, 0)
        send = lax.dynamic_slice_in_dim(x, (1 - bit) * half, half, 0)
        x = keep + swap(send, "lag", mask)
    return x


def all_reduce_src(x):
    for mask in bit_masks("src"):
        x = x + swap(x, "src", mask)
    return x


def all_gather_lag(y):
    for mask in reversed(bit_masks("lag")):
        bit = (lax.axis_index("lag") // mask) % 2
        other = swap(y, "lag", mask)
        first = jnp.where(bit == 0, y, other)
        second = jnp.where(bit == 0, other, y)
        y = jnp.concatenate([first, second], axis=0)
    return y


def ring_distance(a, b, size):
    d = abs(a - b) % size
    return min(d, size - d)


def src_distance(a, b):
    x_size = 4
    hops_x = ring_distance(a % x_size, b % x_size, x_size)
    hops_y = 2 * ring_distance(a // x_size, b // x_size, 2)
    return hops_x + hops_y


def transposed(chunk):
    recv_n = lax.axis_size("recv")
    src_n = lax.axis_size("src")
    route = []
    for s in range(src_n):
        far_first = sorted(range(recv_n), key=lambda r: (-ring_distance(r, s, recv_n), r))
        near_first = sorted(range(src_n), key=lambda q: (src_distance(q, s), q))
        for r, sender in zip(far_first, near_first):
            route.append((s * src_n + sender, r * src_n + s))
    return lax.ppermute(chunk, ("recv", "src"), route)


def friction(stress, offset, background, classes, rate_scale, stress_scale):
    row_total = stress.shape[0]
    element_class = lax.dynamic_slice_in_dim(classes, offset, row_total, 0)
    loaded = lax.dynamic_slice_in_dim(background, offset, row_total, 0)
    selector = (
        element_class[:, None] == jnp.arange(rate_scale.shape[0], dtype=jnp.int32)[None, :]
    ).astype(jnp.float32)
    limit = jnp.sum(selector * rate_scale[None, :], axis=1)[:, None]
    width_scale = jnp.sum(selector * stress_scale[None, :], axis=1)[:, None]
    return (limit * jnp.tanh((loaded + stress) / width_scale)).astype(jnp.bfloat16)


def local(kernel, causal_mask, history, background, classes, rate_scale, stress_scale):
    rows_here, lag_here, cols_here = kernel.shape
    block_size = rows_here // causal_mask.shape[0]
    allowed = jnp.repeat(jnp.repeat(causal_mask, block_size, 0), block_size, 2) > 0
    masked_rows = jnp.where(allowed, kernel, jnp.zeros_like(kernel)).reshape(
        rows_here, lag_here * cols_here
    )
    scenarios = history.shape[2]
    lag_n = lax.axis_size("lag")
    lag_pos = lax.axis_index("lag")
    chunk_rows = rows_here // lag_n
    offset = chunk_offset(lag_pos, rows_here)

    serial = []
    for lag_index in range(SERIAL):
        allowed_here = jnp.repeat(jnp.repeat(causal_mask[:, lag_index, :], block_size, 0), block_size, 1) > 0
        serial.append(jnp.where(allowed_here, kernel[:, lag_index, :], jnp.zeros_like(kernel[:, lag_index, :])))
    serial = jnp.stack(serial).transpose(1, 0, 2).reshape(rows_here, SERIAL * cols_here)
    serial = jnp.where(lag_pos == 0, serial, jnp.zeros_like(serial)).astype(jnp.float32)

    ahead = STEPS - 1
    earlier = lax.ppermute(history[lag_here - ahead:], "lag", [(i, i + 1) for i in range(lag_n - 1)])
    extended = jnp.concatenate([earlier, history], axis=0)
    first = jnp.dot(masked_rows, history.reshape(lag_here * cols_here, scenarios),
                    preferred_element_type=jnp.float32)
    later = []
    for step_index in range(1, STEPS):
        shifted = extended[ahead - step_index: ahead - step_index + lag_here]
        later.append(jnp.dot(masked_rows, shifted.reshape(lag_here * cols_here, scenarios),
                             preferred_element_type=jnp.float32))
    later = reduce_scatter_lag(jnp.concatenate(later + [serial], axis=1))
    own = later[:, (STEPS - 1) * scenarios:].astype(kernel.dtype)
    own = own.reshape(chunk_rows, SERIAL, cols_here).transpose(1, 0, 2)
    known = [reduce_scatter_lag(first)] + [
        later[:, (t - 1) * scenarios: t * scenarios] for t in range(1, STEPS)
    ]

    outputs = []
    sources = []
    for step_index in range(STEPS):
        partial = known[step_index]
        for lag_index in range(min(step_index, SERIAL)):
            partial = partial + jnp.dot(own[lag_index], sources[step_index - 1 - lag_index],
                                        preferred_element_type=jnp.float32)
        total = all_reduce_src(partial)
        rates_chunk = friction(total, offset, background, classes, rate_scale, stress_scale)
        if step_index + 1 < STEPS:
            block = all_gather_lag(transposed(rates_chunk))
            sources.append(block)
        outputs.append(all_gather_lag(rates_chunk))
    return jnp.stack(outputs)


def solution(mesh):
    in_specs = (
        P("recv", "lag", "src"),
        P("recv", "lag", "src"),
        P("lag", "src", None),
        P("recv", None),
        P("recv"),
        P(),
        P(),
    )
    out_specs = P(None, "recv", None)
    return jax.shard_map(local, mesh=mesh, in_specs=in_specs, out_specs=out_specs, check_vma=False)
```

```python
import jax
import jax.numpy as jnp
from jax import lax
from jax.sharding import PartitionSpec as P

STEPS = 3
SERIAL = 2


def bit_masks(axis):
    masks = []
    mask = 1
    while mask < lax.axis_size(axis):
        masks.append(mask)
        mask *= 2
    return masks


def swap(block, axis, mask):
    size = lax.axis_size(axis)
    return lax.ppermute(block, axis, [(i, i ^ mask) for i in range(size)])


def chunk_offset(lag_pos, rows):
    offset = 0
    for mask in bit_masks("lag"):
        rows = rows // 2
        offset = offset + ((lag_pos // mask) % 2) * rows
    return offset


def reduce_scatter_lag(x):
    for mask in bit_masks("lag"):
        half = x.shape[0] // 2
        bit = (lax.axis_index("lag") // mask) % 2
        keep = lax.dynamic_slice_in_dim(x, bit * half, half, 0)
        send = lax.dynamic_slice_in_dim(x, (1 - bit) * half, half, 0)
        x = keep + swap(send, "lag", mask)
    return x


def all_reduce_src(x):
    for mask in bit_masks("src"):
        x = x + swap(x, "src", mask)
    return x


def all_gather_lag(y):
    for mask in reversed(bit_masks("lag")):
        bit = (lax.axis_index("lag") // mask) % 2
        other = swap(y, "lag", mask)
        first = jnp.where(bit == 0, y, other)
        second = jnp.where(bit == 0, other, y)
        y = jnp.concatenate([first, second], axis=0)
    return y


def ring_distance(a, b, size):
    d = abs(a - b) % size
    return min(d, size - d)


def src_distance(a, b):
    x_size = 4
    hops_x = ring_distance(a % x_size, b % x_size, x_size)
    hops_y = 2 * ring_distance(a // x_size, b // x_size, 2)
    return hops_x + hops_y


def transposed(chunk):
    recv_n = lax.axis_size("recv")
    src_n = lax.axis_size("src")
    route = []
    for s in range(src_n):
        far_first = sorted(range(recv_n), key=lambda r: (-ring_distance(r, s, recv_n), r))
        near_first = sorted(range(src_n), key=lambda q: (src_distance(q, s), q))
        for r, sender in zip(far_first, near_first):
            route.append((s * src_n + sender, r * src_n + s))
    return lax.ppermute(chunk, ("recv", "src"), route)


def friction(stress, offset, background, classes, rate_scale, stress_scale):
    row_total = stress.shape[0]
    element_class = lax.dynamic_slice_in_dim(classes, offset, row_total, 0)
    loaded = lax.dynamic_slice_in_dim(background, offset, row_total, 0)
    selector = (
        element_class[:, None] == jnp.arange(rate_scale.shape[0], dtype=jnp.int32)[None, :]
    ).astype(jnp.float32)
    limit = jnp.sum(selector * rate_scale[None, :], axis=1)[:, None]
    width_scale = jnp.sum(selector * stress_scale[None, :], axis=1)[:, None]
    return (limit * jnp.tanh((loaded + stress) / width_scale)).astype(jnp.bfloat16)


def local(kernel, causal_mask, history, background, classes, rate_scale, stress_scale):
    rows_here, lag_here, cols_here = kernel.shape
    block_size = rows_here // causal_mask.shape[0]
    allowed = jnp.repeat(jnp.repeat(causal_mask, block_size, 0), block_size, 2) > 0
    masked_rows = jnp.where(allowed, kernel, jnp.zeros_like(kernel)).reshape(
        rows_here, lag_here * cols_here
    )
    scenarios = history.shape[2]
    lag_n = lax.axis_size("lag")
    lag_pos = lax.axis_index("lag")
    chunk_rows = rows_here // lag_n
    offset = chunk_offset(lag_pos, rows_here)

    serial = []
    for lag_index in range(SERIAL):
        allowed_here = jnp.repeat(jnp.repeat(causal_mask[:, lag_index, :], block_size, 0), block_size, 1) > 0
        serial.append(jnp.where(allowed_here, kernel[:, lag_index, :], jnp.zeros_like(kernel[:, lag_index, :])))
    serial = jnp.stack(serial)
    def rows_of(targets):
        starts = [chunk_offset(t, rows_here) for t in targets]
        return jnp.concatenate([serial[:, a:a + chunk_rows] for a in starts], axis=1)

    far, near = lag_n // 2, 1
    far_side = rows_of([far, far + near])
    arrived = lax.ppermute(far_side, "lag", [(0, far)])
    held = jnp.where(lag_pos == far, arrived, far_side)
    passed = jnp.where(lag_pos == 0, rows_of([near]), held[:, chunk_rows:])
    arrived = lax.ppermute(passed, "lag", [(0, near), (far, far + near)])
    own = jnp.where(lag_pos == 0, rows_of([0]), jnp.where(lag_pos == far, held[:, :chunk_rows], arrived))

    ahead = STEPS - 1
    earlier = lax.ppermute(history[lag_here - ahead:], "lag", [(i, i + 1) for i in range(lag_n - 1)])
    extended = jnp.concatenate([earlier, history], axis=0)
    first = jnp.dot(masked_rows, history.reshape(lag_here * cols_here, scenarios),
                    preferred_element_type=jnp.float32)
    later = []
    for step_index in range(1, STEPS):
        shifted = extended[ahead - step_index: ahead - step_index + lag_here]
        later.append(jnp.dot(masked_rows, shifted.reshape(lag_here * cols_here, scenarios),
                             preferred_element_type=jnp.float32))
    later = reduce_scatter_lag(jnp.concatenate(later, axis=1))
    known = [reduce_scatter_lag(first)] + [
        later[:, (t - 1) * scenarios: t * scenarios] for t in range(1, STEPS)
    ]

    outputs = []
    sources = []
    for step_index in range(STEPS):
        partial = known[step_index]
        for lag_index in range(min(step_index, SERIAL)):
            partial = partial + jnp.dot(own[lag_index], sources[step_index - 1 - lag_index],
                                        preferred_element_type=jnp.float32)
        total = all_reduce_src(partial)
        rates_chunk = friction(total, offset, background, classes, rate_scale, stress_scale)
        if step_index + 1 < STEPS:
            block = all_gather_lag(transposed(rates_chunk))
            sources.append(block)
        outputs.append(all_gather_lag(rates_chunk))
    return jnp.stack(outputs)


def solution(mesh):
    in_specs = (
        P("recv", "lag", "src"),
        P("recv", "lag", "src"),
        P("lag", "src", None),
        P("recv", None),
        P("recv"),
        P(),
        P(),
    )
    out_specs = P(None, "recv", None)
    return jax.shard_map(local, mesh=mesh, in_specs=in_specs, out_specs=out_specs, check_vma=False)
```

```python
import jax
import jax.numpy as jnp
from jax import lax
from jax.sharding import PartitionSpec as P

STEPS = 3
SERIAL = 2


def bit_masks(axis):
    masks = []
    mask = 1
    while mask < lax.axis_size(axis):
        masks.append(mask)
        mask *= 2
    return masks


def swap(block, axis, mask):
    size = lax.axis_size(axis)
    return lax.ppermute(block, axis, [(i, i ^ mask) for i in range(size)])


def chunk_offset(lag_pos, rows):
    offset = 0
    for mask in bit_masks("lag"):
        rows = rows // 2
        offset = offset + ((lag_pos // mask) % 2) * rows
    return offset


def reduce_scatter_lag(x):
    for mask in bit_masks("lag"):
        half = x.shape[0] // 2
        bit = (lax.axis_index("lag") // mask) % 2
        keep = lax.dynamic_slice_in_dim(x, bit * half, half, 0)
        send = lax.dynamic_slice_in_dim(x, (1 - bit) * half, half, 0)
        x = keep + swap(send, "lag", mask)
    return x


def all_reduce_src(x):
    for mask in bit_masks("src"):
        x = x + swap(x, "src", mask)
    return x


def all_gather_lag(y):
    for mask in reversed(bit_masks("lag")):
        bit = (lax.axis_index("lag") // mask) % 2
        other = swap(y, "lag", mask)
        first = jnp.where(bit == 0, y, other)
        second = jnp.where(bit == 0, other, y)
        y = jnp.concatenate([first, second], axis=0)
    return y


def ring_distance(a, b, size):
    d = abs(a - b) % size
    return min(d, size - d)


def src_distance(a, b):
    x_size = 4
    hops_x = ring_distance(a % x_size, b % x_size, x_size)
    hops_y = 2 * ring_distance(a // x_size, b // x_size, 2)
    return hops_x + hops_y


def sources_of(chunk, rows_total):
    lag_n = lax.axis_size("lag")
    recv_n = lax.axis_size("recv")
    src_n = lax.axis_size("src")
    lag_pos = lax.axis_index("lag")
    senders = {}
    for s in range(src_n):
        far_first = sorted(range(recv_n), key=lambda r: (-ring_distance(r, s, recv_n), r))
        near_first = sorted(range(src_n), key=lambda q: (src_distance(q, s), q))
        for r, sender in zip(far_first, near_first):
            senders[(r, s)] = sender
    block = jnp.zeros((rows_total,) + chunk.shape[1:], chunk.dtype)
    for shift in range(lag_n):
        route = []
        for g in range(lag_n):
            for (r, s), sender in senders.items():
                source = (((g - shift) % lag_n) * recv_n + s) * src_n + sender
                route.append((source, (g * recv_n + r) * src_n + s))
        piece = lax.ppermute(chunk, ("lag", "recv", "src"), route)
        owner = (lag_pos - shift) % lag_n
        block = lax.dynamic_update_slice_in_dim(block, piece, chunk_offset(owner, rows_total), 0)
    return block


def friction(stress, offset, background, classes, rate_scale, stress_scale):
    row_total = stress.shape[0]
    element_class = lax.dynamic_slice_in_dim(classes, offset, row_total, 0)
    loaded = lax.dynamic_slice_in_dim(background, offset, row_total, 0)
    selector = (
        element_class[:, None] == jnp.arange(rate_scale.shape[0], dtype=jnp.int32)[None, :]
    ).astype(jnp.float32)
    limit = jnp.sum(selector * rate_scale[None, :], axis=1)[:, None]
    width_scale = jnp.sum(selector * stress_scale[None, :], axis=1)[:, None]
    return (limit * jnp.tanh((loaded + stress) / width_scale)).astype(jnp.bfloat16)


def local(kernel, causal_mask, history, background, classes, rate_scale, stress_scale):
    rows_here, lag_here, cols_here = kernel.shape
    block_size = rows_here // causal_mask.shape[0]
    allowed = jnp.repeat(jnp.repeat(causal_mask, block_size, 0), block_size, 2) > 0
    masked_rows = jnp.where(allowed, kernel, jnp.zeros_like(kernel)).reshape(
        rows_here, lag_here * cols_here
    )
    scenarios = history.shape[2]
    lag_n = lax.axis_size("lag")
    lag_pos = lax.axis_index("lag")
    chunk_rows = rows_here // lag_n
    offset = chunk_offset(lag_pos, rows_here)

    serial = []
    for lag_index in range(SERIAL):
        allowed_here = jnp.repeat(jnp.repeat(causal_mask[:, lag_index, :], block_size, 0), block_size, 1) > 0
        serial.append(jnp.where(allowed_here, kernel[:, lag_index, :], jnp.zeros_like(kernel[:, lag_index, :])))
    serial = jnp.stack(serial)
    own = lax.dynamic_slice_in_dim(serial, offset, chunk_rows, 1)
    for target in range(1, lag_n):
        start = chunk_offset(target, rows_here)
        arrived = lax.ppermute(serial[:, start:start + chunk_rows], "lag", [(0, target)])
        own = jnp.where(lag_pos == target, arrived, own)

    ahead = STEPS - 1
    earlier = lax.ppermute(history[lag_here - ahead:], "lag", [(i, i + 1) for i in range(lag_n - 1)])
    extended = jnp.concatenate([earlier, history], axis=0)
    first = jnp.dot(masked_rows, history.reshape(lag_here * cols_here, scenarios),
                    preferred_element_type=jnp.float32)
    later = []
    for step_index in range(1, STEPS):
        shifted = extended[ahead - step_index: ahead - step_index + lag_here]
        later.append(jnp.dot(masked_rows, shifted.reshape(lag_here * cols_here, scenarios),
                             preferred_element_type=jnp.float32))
    later = reduce_scatter_lag(jnp.concatenate(later, axis=1))
    known = [reduce_scatter_lag(first)] + [
        later[:, (t - 1) * scenarios: t * scenarios] for t in range(1, STEPS)
    ]

    outputs = []
    sources = []
    for step_index in range(STEPS):
        partial = known[step_index]
        for lag_index in range(min(step_index, SERIAL)):
            partial = partial + jnp.dot(own[lag_index], sources[step_index - 1 - lag_index],
                                        preferred_element_type=jnp.float32)
        total = all_reduce_src(partial)
        rates_chunk = friction(total, offset, background, classes, rate_scale, stress_scale)
        if step_index + 1 < STEPS:
            block = sources_of(rates_chunk, rows_here)
            sources.append(block)
        outputs.append(all_gather_lag(rates_chunk))
    return jnp.stack(outputs)


def solution(mesh):
    in_specs = (
        P("recv", "lag", "src"),
        P("recv", "lag", "src"),
        P("lag", "src", None),
        P("recv", None),
        P("recv"),
        P(),
        P(),
    )
    out_specs = P(None, "recv", None)
    return jax.shard_map(local, mesh=mesh, in_specs=in_specs, out_specs=out_specs, check_vma=False)
```

```python
import jax
import jax.numpy as jnp
from jax import lax
from jax.sharding import PartitionSpec as P

STEPS = 3
SERIAL = 2


def bit_masks(axis):
    masks = []
    mask = 1
    while mask < lax.axis_size(axis):
        masks.append(mask)
        mask *= 2
    return masks


def swap(block, axis, mask):
    size = lax.axis_size(axis)
    return lax.ppermute(block, axis, [(i, i ^ mask) for i in range(size)])


def chunk_offset(lag_pos, rows):
    offset = 0
    for mask in bit_masks("lag"):
        rows = rows // 2
        offset = offset + ((lag_pos // mask) % 2) * rows
    return offset


def reduce_scatter_lag(x):
    for mask in bit_masks("lag"):
        half = x.shape[0] // 2
        bit = (lax.axis_index("lag") // mask) % 2
        keep = lax.dynamic_slice_in_dim(x, bit * half, half, 0)
        send = lax.dynamic_slice_in_dim(x, (1 - bit) * half, half, 0)
        x = keep + swap(send, "lag", mask)
    return x


def all_reduce_src(x):
    for mask in bit_masks("src"):
        x = x + swap(x, "src", mask)
    return x


def all_gather_lag(y, axis=0):
    for mask in reversed(bit_masks("lag")):
        bit = (lax.axis_index("lag") // mask) % 2
        other = swap(y, "lag", mask)
        first = jnp.where(bit == 0, y, other)
        second = jnp.where(bit == 0, other, y)
        y = jnp.concatenate([first, second], axis=axis)
    return y


def ring_distance(a, b, size):
    d = abs(a - b) % size
    return min(d, size - d)


def src_distance(a, b):
    x_size = 4
    hops_x = ring_distance(a % x_size, b % x_size, x_size)
    hops_y = 2 * ring_distance(a // x_size, b // x_size, 2)
    return hops_x + hops_y


def transposed(chunk):
    recv_n = lax.axis_size("recv")
    src_n = lax.axis_size("src")
    route = []
    for s in range(src_n):
        far_first = sorted(range(recv_n), key=lambda r: (-ring_distance(r, s, recv_n), r))
        near_first = sorted(range(src_n), key=lambda q: (src_distance(q, s), q))
        for r, sender in zip(far_first, near_first):
            route.append((s * src_n + sender, r * src_n + s))
    return lax.ppermute(chunk, ("recv", "src"), route)


def friction(stress, offset, background, classes, rate_scale, stress_scale):
    row_total = stress.shape[0]
    element_class = lax.dynamic_slice_in_dim(classes, offset, row_total, 0)
    loaded = lax.dynamic_slice_in_dim(background, offset, row_total, 0)
    selector = (
        element_class[:, None] == jnp.arange(rate_scale.shape[0], dtype=jnp.int32)[None, :]
    ).astype(jnp.float32)
    limit = jnp.sum(selector * rate_scale[None, :], axis=1)[:, None]
    width_scale = jnp.sum(selector * stress_scale[None, :], axis=1)[:, None]
    return (limit * jnp.tanh((loaded + stress) / width_scale)).astype(jnp.bfloat16)


def local(kernel, causal_mask, history, background, classes, rate_scale, stress_scale):
    rows_here, lag_here, cols_here = kernel.shape
    block_size = rows_here // causal_mask.shape[0]
    allowed = jnp.repeat(jnp.repeat(causal_mask, block_size, 0), block_size, 2) > 0
    masked_rows = jnp.where(allowed, kernel, jnp.zeros_like(kernel)).reshape(
        rows_here, lag_here * cols_here
    )
    scenarios = history.shape[2]
    lag_n = lax.axis_size("lag")
    lag_pos = lax.axis_index("lag")
    chunk_rows = rows_here // lag_n
    offset = chunk_offset(lag_pos, rows_here)

    serial = []
    for lag_index in range(SERIAL):
        allowed_here = jnp.repeat(jnp.repeat(causal_mask[:, lag_index, :], block_size, 0), block_size, 1) > 0
        serial.append(jnp.where(allowed_here, kernel[:, lag_index, :], jnp.zeros_like(kernel[:, lag_index, :])))
    serial = jnp.stack(serial)
    own = lax.dynamic_slice_in_dim(serial, offset, chunk_rows, 1)
    for target in range(1, lag_n):
        start = chunk_offset(target, rows_here)
        arrived = lax.ppermute(serial[:, start:start + chunk_rows], "lag", [(0, target)])
        own = jnp.where(lag_pos == target, arrived, own)

    ahead = STEPS - 1
    earlier = lax.ppermute(history[lag_here - ahead:], "lag", [(i, i + 1) for i in range(lag_n - 1)])
    extended = jnp.concatenate([earlier, history], axis=0)
    first = jnp.dot(masked_rows, history.reshape(lag_here * cols_here, scenarios),
                    preferred_element_type=jnp.float32)
    later = []
    for step_index in range(1, STEPS):
        shifted = extended[ahead - step_index: ahead - step_index + lag_here]
        later.append(jnp.dot(masked_rows, shifted.reshape(lag_here * cols_here, scenarios),
                             preferred_element_type=jnp.float32))
    later = reduce_scatter_lag(jnp.concatenate(later, axis=1))
    known = [reduce_scatter_lag(first)] + [
        later[:, (t - 1) * scenarios: t * scenarios] for t in range(1, STEPS)
    ]

    outputs = []
    sources = []
    for step_index in range(STEPS):
        partial = known[step_index]
        for lag_index in range(min(step_index, SERIAL)):
            partial = partial + jnp.dot(own[lag_index], sources[step_index - 1 - lag_index],
                                        preferred_element_type=jnp.float32)
        total = all_reduce_src(partial)
        rates_chunk = friction(total, offset, background, classes, rate_scale, stress_scale)
        if step_index + 1 < STEPS:
            block = all_gather_lag(transposed(rates_chunk))
            sources.append(block)
        outputs.append(rates_chunk)
    return all_gather_lag(jnp.stack(outputs), axis=1)


def solution(mesh):
    in_specs = (
        P("recv", "lag", "src"),
        P("recv", "lag", "src"),
        P("lag", "src", None),
        P("recv", None),
        P("recv"),
        P(),
        P(),
    )
    out_specs = P(None, "recv", None)
    return jax.shard_map(local, mesh=mesh, in_specs=in_specs, out_specs=out_specs, check_vma=False)
```

```python
import jax
import jax.numpy as jnp
from jax import lax
from jax.sharding import PartitionSpec as P

STEPS = 3
SERIAL = 2


def bit_masks(axis):
    masks = []
    mask = 1
    while mask < lax.axis_size(axis):
        masks.append(mask)
        mask *= 2
    return masks


def swap(block, axis, mask):
    size = lax.axis_size(axis)
    return lax.ppermute(block, axis, [(i, i ^ mask) for i in range(size)])


def chunk_offset(lag_pos, rows):
    offset = 0
    for mask in bit_masks("lag"):
        rows = rows // 2
        offset = offset + ((lag_pos // mask) % 2) * rows
    return offset


def reduce_scatter_lag(x):
    for mask in bit_masks("lag"):
        half = x.shape[0] // 2
        bit = (lax.axis_index("lag") // mask) % 2
        keep = lax.dynamic_slice_in_dim(x, bit * half, half, 0)
        send = lax.dynamic_slice_in_dim(x, (1 - bit) * half, half, 0)
        x = keep + swap(send, "lag", mask)
    return x


def all_reduce_src(x):
    for mask in bit_masks("src"):
        x = x + swap(x, "src", mask)
    return x


def all_gather_lag(y, axis=0):
    for mask in reversed(bit_masks("lag")):
        bit = (lax.axis_index("lag") // mask) % 2
        other = swap(y, "lag", mask)
        first = jnp.where(bit == 0, y, other)
        second = jnp.where(bit == 0, other, y)
        y = jnp.concatenate([first, second], axis=axis)
    return y


def ring_distance(a, b, size):
    d = abs(a - b) % size
    return min(d, size - d)


def src_distance(a, b):
    x_size = 4
    hops_x = ring_distance(a % x_size, b % x_size, x_size)
    hops_y = 2 * ring_distance(a // x_size, b // x_size, 2)
    return hops_x + hops_y


def transposed(chunk):
    recv_n = lax.axis_size("recv")
    src_n = lax.axis_size("src")
    route = []
    for s in range(src_n):
        far_first = sorted(range(recv_n), key=lambda r: (-ring_distance(r, s, recv_n), r))
        near_first = sorted(range(src_n), key=lambda q: (src_distance(q, s), q))
        for r, sender in zip(far_first, near_first):
            route.append((s * src_n + sender, r * src_n + s))
    return lax.ppermute(chunk, ("recv", "src"), route)


def friction(stress, offset, background, classes, rate_scale, stress_scale):
    row_total = stress.shape[0]
    element_class = lax.dynamic_slice_in_dim(classes, offset, row_total, 0)
    loaded = lax.dynamic_slice_in_dim(background, offset, row_total, 0)
    selector = (
        element_class[:, None] == jnp.arange(rate_scale.shape[0], dtype=jnp.int32)[None, :]
    ).astype(jnp.float32)
    limit = jnp.sum(selector * rate_scale[None, :], axis=1)[:, None]
    width_scale = jnp.sum(selector * stress_scale[None, :], axis=1)[:, None]
    return (limit * jnp.tanh((loaded + stress) / width_scale)).astype(jnp.bfloat16)


def local(kernel, causal_mask, history, background, classes, rate_scale, stress_scale):
    rows_here, lag_here, cols_here = kernel.shape
    block_size = rows_here // causal_mask.shape[0]
    allowed = jnp.repeat(jnp.repeat(causal_mask, block_size, 0), block_size, 2) > 0
    masked_rows = jnp.where(allowed, kernel, jnp.zeros_like(kernel)).reshape(
        rows_here, lag_here * cols_here
    )
    scenarios = history.shape[2]
    lag_n = lax.axis_size("lag")
    lag_pos = lax.axis_index("lag")
    chunk_rows = rows_here // lag_n
    offset = chunk_offset(lag_pos, rows_here)

    serial = []
    for lag_index in range(SERIAL):
        allowed_here = jnp.repeat(jnp.repeat(causal_mask[:, lag_index, :], block_size, 0), block_size, 1) > 0
        serial.append(jnp.where(allowed_here, kernel[:, lag_index, :], jnp.zeros_like(kernel[:, lag_index, :])))
    serial = jnp.stack(serial)
    own = lax.dynamic_slice_in_dim(serial, offset, chunk_rows, 1)
    for target in range(1, lag_n):
        start = chunk_offset(target, rows_here)
        arrived = lax.ppermute(serial[:, start:start + chunk_rows], "lag", [(0, target)])
        own = jnp.where(lag_pos == target, arrived, own)

    ahead = STEPS - 1
    earlier = lax.ppermute(history[lag_here - ahead:], "lag", [(i, i + 1) for i in range(lag_n - 1)])
    extended = jnp.concatenate([earlier, history], axis=0)
    first = jnp.dot(masked_rows, history.reshape(lag_here * cols_here, scenarios),
                    preferred_element_type=jnp.float32)
    later = []
    for step_index in range(1, STEPS):
        shifted = extended[ahead - step_index: ahead - step_index + lag_here]
        later.append(jnp.dot(masked_rows, shifted.reshape(lag_here * cols_here, scenarios),
                             preferred_element_type=jnp.float32))
    later = reduce_scatter_lag(jnp.concatenate(later, axis=1))
    known = [reduce_scatter_lag(first)] + [
        later[:, (t - 1) * scenarios: t * scenarios] for t in range(1, STEPS)
    ]

    outputs = []
    sources = []
    for step_index in range(STEPS):
        partial = known[step_index]
        for lag_index in range(min(step_index, SERIAL)):
            partial = partial + jnp.dot(own[lag_index], sources[step_index - 1 - lag_index],
                                        preferred_element_type=jnp.float32)
        total = all_reduce_src(partial)
        rates_chunk = friction(total, offset, background, classes, rate_scale, stress_scale)
        if step_index + 1 < STEPS:
            block = all_gather_lag(transposed(rates_chunk))
            sources.append(block)
        outputs.append(rates_chunk)
    earlier_steps = all_gather_lag(jnp.stack(outputs[:-1]), axis=1)
    return jnp.concatenate([earlier_steps, all_gather_lag(outputs[-1])[None]], axis=0)


def solution(mesh):
    in_specs = (
        P("recv", "lag", "src"),
        P("recv", "lag", "src"),
        P("lag", "src", None),
        P("recv", None),
        P("recv"),
        P(),
        P(),
    )
    out_specs = P(None, "recv", None)
    return jax.shard_map(local, mesh=mesh, in_specs=in_specs, out_specs=out_specs, check_vma=False)
```
